256 devices in a mesh: dp: 8 (over x, core), expert: 16 (over y, z_hi), tensor: 2 (over z_lo).
Axes of the slice: x: 4, y: 4, z: 8 (z_hi: 4, z_lo: 2; z = z_hi * 2 + z_lo), core: 2. Of those that a mesh axis runs over, the one named last changes fastest.
Arguments:
- tokens: bfloat16 [1024, 7168], P(('dp', 'expert'), 'tensor'), may hold values from -6 to 6
- upstream: bfloat16 [1024, 7168], P(('dp', 'expert'), 'tensor'), may hold values from -3 to 3
- probs: bfloat16 [1024, 8], P(('dp', 'expert')), may hold values from 0.049804688 to 0.59765625
- routing: int32 [1024, 8], P(('dp', 'expert')), may hold values from 0 to 15, all different within a row; in each aligned block of 8 rows (0 to 7, 8 to 15, ...) at most 5 rows name the same one
- row_rollout: int32 [1024], P(('dp', 'expert')), may hold values from 0 to 255
- group_ids: int32 [256], replicated, may hold values from 0 to 31
- rewards: int32 [256], replicated, may hold values from 0 to 1
- w_gate: bfloat16 [16, 7168, 2048], P('expert', None, ('dp', 'tensor')), may hold values from -0.0625 to 0.0625
- w_up: bfloat16 [16, 7168, 2048], P('expert', None, ('dp', 'tensor')), may hold values from -0.0625 to 0.0625
- w_down: bfloat16 [16, 2048, 7168], P('expert', ('dp', 'tensor')), may hold values from -0.125 to 0.125
Outputs:
- input_grad: bfloat16 [1024, 7168], P(('dp', 'expert'), 'tensor')
- route_grad: bfloat16 [1024, 8], P(('dp', 'expert'))
- grad_gate: bfloat16 [16, 7168, 2048], P('expert', None, ('dp', 'tensor'))
- grad_up: bfloat16 [16, 7168, 2048], P('expert', None, ('dp', 'tensor'))
- grad_down: bfloat16 [16, 2048, 7168], P('expert', ('dp', 'tensor'))
The draws below stay inside these ranges and needn't reach their ends.
Inputs may be any that keep to these rules, and one draw needn't show every extreme that they name: `routing`: each row names 8 different experts. Within each aligned block of 8 rows (the tokens of one index pair of dp and expert) no expert is named by more than 5 rows, a bound that some block reaches.
All inputs are finite; a program needn't handle non-finite values.
Results may differ from the reference program's by a relative error of at most 0.025.
Values may be sent and summed in bfloat16 or wider, within the bound.
No kernel may reach another device: no remote copies, remote signals or barrier semaphores. Data moves between devices by JAX's collectives and lax.ppermute only.
A program may use at most 128 MiB of HBM per device.

```python
import math
import jax
import jax.numpy as jnp
import numpy as np
from jax import lax

D = 7168
FF = 2048
TOP = 8
TOK_GRP = 8
ROLLOUTS = 256
GROUPS = 32
EXPERTS = 16
CAP = 5
TOKENS = 1024
N_DP = 8
N_TENSOR = 2


def plant(array, stream_key, low, largest):
    index_at = [jax.random.randint(jax.random.fold_in(stream_key, axis), (), 0, length) for axis, length in enumerate(array.shape)]
    main_axis = array.shape.index(max(array.shape))
    beside = index_at[:main_axis] + [(index_at[main_axis] + 1) % array.shape[main_axis]] + index_at[main_axis + 1:]
    return array.at[tuple(index_at)].set(low).at[tuple(beside)].set(largest)


def shard_levels(rng, shape, cuts, smallest, top_value):
    loudness, own = 1.0, jax.random.fold_in(rng, 6)
    for position, shards_of in cuts:
        draws = jnp.exp(jax.random.uniform(jax.random.fold_in(own, position), (shards_of,), jnp.float32, smallest / len(cuts), top_value / len(cuts)))
        loudness = loudness * jnp.repeat(draws, shape[position] // shards_of).reshape([-1 if axis == position else 1 for axis in range(len(shape))])
    return loudness


def shared_out(own_key, own, number, rows, number_of, top, reach, slope):
    ranking = jax.random.permutation(own_key, number_of)
    heavy_load, common = portions_of(number_of, rows * top, reach, slope, True), portions_of(number_of, rows * top, reach, slope, False)
    places = jnp.arange(number_of)

    def named(tallies, rotation):
        used = int((tallies > 0).sum())
        fixed = max(1, used // 4)
        passed = fixed + (places - fixed + rotation * (used - fixed)) % max(1, number_of - fixed)
        return jnp.zeros((number_of,), jnp.int32).at[ranking[jnp.where(places < fixed, places, passed)]].set(jnp.asarray(tallies, jnp.int32))

    tallies = jnp.where(number % 4 == 0, named(heavy_load, number // 4), named(common, number - number // 4 - 1))
    mixed = jax.random.permutation(jax.random.fold_in(own, 3), number_of)
    donor, receiver = mixed[0:number_of // 2 * 2:2], mixed[1:number_of // 2 * 2:2]
    slack = jnp.minimum(tallies[donor] - 1, reach - tallies[receiver]) // 2
    slack = jnp.where((donor == ranking[0]) | (receiver == ranking[0]) | (tallies[receiver] == 0), 0, jnp.maximum(slack, 0))
    passed = jax.random.randint(jax.random.fold_in(own, 4), (number_of // 2,), 0, 1 << 20) % (slack + 1)
    tallies = tallies.at[donor].add(-passed).at[receiver].add(passed)
    labels = jnp.searchsorted(jnp.cumsum(tallies), jnp.arange(rows * top), side="right").astype(jnp.int32)
    listing = labels.reshape(top, rows).T
    listing = listing[jax.random.permutation(jax.random.fold_in(own, 1), rows)]
    rotation = jax.random.randint(jax.random.fold_in(own, 2), (rows, 1), 0, top)
    return jnp.take_along_axis(listing, (jnp.arange(top)[None, :] + rotation) % top, axis=1)


def portions_of(amount, total, limit, skew, full):
    loads = [(1 << 20) // math.isqrt(grade ** skew) + 1 for grade in range(1, amount + 1)]
    largest = limit if full else min(limit, max(-(-total // amount), total * loads[0] // sum(loads)))
    least = 1 if total - largest >= amount - 1 else 0
    counts, surplus = [largest] + [least] * (amount - 1), total - largest - least * (amount - 1)
    while surplus > 0:
        candidates = [i for i in range(1, amount) if counts[i] < largest] or [i for i in range(1, amount) if counts[i] < limit]
        mass, left = sum([loads[i] for i in candidates]), surplus
        for i in candidates:
            extra = min(limit - counts[i], max(1, left * loads[i] // mass), surplus)
            counts[i] = counts[i] + extra
            surplus = surplus - extra
    return np.array(counts)


def gaussian(rng, shape, spread, limit, shards=(), kind=jnp.bfloat16):
    entries = jax.random.normal(rng, shape, jnp.float32) * spread
    if len(shards) > 0:
        entries = shard_levels(rng, shape, shards, -0.22, 0.18) * entries
    return jnp.clip(entries, min=-limit, max=limit).astype(kind)


def setup_inputs(seed: int = 0) -> dict:
    key_list = jax.random.split(jax.random.key(seed), 11)
    tokens = gaussian(key_list[0], (TOKENS, D), 1.0, 6.0, ((0, 128), (1, 2)))
    upstream = gaussian(key_list[1], (TOKENS, D), 0.5, 3.0, ((0, 128), (1, 2)))
    probs = jnp.clip(0.049804688 + 0.54785156 * jax.random.uniform(key_list[2], (TOKENS, TOP), jnp.float32) ** shard_levels(key_list[2], (TOKENS, TOP), ((0, 128),), -0.2, 0.2), 0.049804688, 0.59765625).astype(jnp.bfloat16)
    routing_keys = jax.random.split(jax.random.fold_in(key_list[3], 1), TOKENS // TOK_GRP)
    routing_turns = jax.random.permutation(jax.random.fold_in(key_list[3], 3), TOKENS // TOK_GRP)
    routing = jax.vmap(lambda own, number: shared_out(jax.random.fold_in(key_list[3], 2), own, number, TOK_GRP, EXPERTS, TOP, CAP, 2))(routing_keys, routing_turns).reshape((TOKENS, TOP))
    row_rollout = plant(jax.random.randint(key_list[4], (TOKENS,), 0, ROLLOUTS), jax.random.fold_in(key_list[4], 1), 0, ROLLOUTS - 1).astype(jnp.int32)
    group_ids = plant(jax.random.randint(key_list[5], (ROLLOUTS,), 0, GROUPS), jax.random.fold_in(key_list[5], 1), 0, GROUPS - 1).astype(jnp.int32)
    rewards = plant(jax.random.randint(key_list[6], (ROLLOUTS,), 0, 2), jax.random.fold_in(key_list[6], 1), 0, 1).astype(jnp.int32)
    w_gate = gaussian(key_list[7], (EXPERTS, D, FF), D ** -0.5, 0.0625, ((0, 16), (2, 16)))
    w_up = gaussian(key_list[8], (EXPERTS, D, FF), D ** -0.5, 0.0625, ((0, 16), (2, 16)))
    w_down = gaussian(key_list[9], (EXPERTS, FF, D), FF ** -0.5, 0.125, ((0, 16), (1, 16)))
    return {"tokens": tokens, "upstream": upstream, "probs": probs, "routing": routing, "row_rollout": row_rollout, "group_ids": group_ids, "rewards": rewards, "w_gate": w_gate, "w_up": w_up, "w_down": w_down}


def advantages(row_rollout, group_ids, rewards):
    same_group = (group_ids[:, None] == group_ids[None, :]).astype(jnp.float32)
    reward_values = rewards.astype(jnp.float32)
    group_total = jnp.dot(same_group, reward_values, precision=lax.Precision.HIGHEST)
    group_count = jnp.sum(same_group, axis=1)
    per_rollout = reward_values - group_total / group_count
    member = (row_rollout[:, None] == jnp.arange(per_rollout.shape[0], dtype=jnp.int32)[None, :]).astype(jnp.float32)
    return jnp.dot(member, per_rollout, precision=lax.Precision.HIGHEST)


def slot_table(route_table, prob_table, expert):
    route_hits = (route_table == expert).astype(jnp.float32)
    occupied = jnp.sum(route_hits, axis=-1)
    weight = jnp.sum(route_hits * prob_table.astype(jnp.float32), axis=-1)
    before = jnp.cumsum(occupied, axis=1) - occupied
    slot_index = jnp.arange(CAP, dtype=jnp.float32)
    chosen = occupied[:, None, :] * (before[:, None, :] == slot_index[None, :, None]).astype(jnp.float32)
    return route_hits, weight, chosen


def reference(tokens, upstream, probs, routing, row_rollout, group_ids, rewards, w_gate, w_up, w_down):
    highest = lax.Precision.HIGHEST
    advantage = advantages(row_rollout, group_ids, rewards)
    cotangent = (advantage[:, None] * upstream.astype(jnp.float32)).astype(jnp.bfloat16)
    groups = TOKENS // TOK_GRP
    blocks = N_DP * N_TENSOR
    width = FF // blocks
    token_rows = tokens.astype(jnp.float32).reshape(groups, TOK_GRP, D)
    back_rows = cotangent.astype(jnp.float32).reshape(groups, TOK_GRP, D)
    route_table = routing.reshape(groups, TOK_GRP, TOP)
    prob_table = probs.reshape(groups, TOK_GRP, TOP)

    def one_expert(packed):
        expert, gate_weight, up_weight, down_weight = packed
        route_hits, weight, chosen = slot_table(route_table, prob_table, expert)
        rows_in = jnp.einsum('gcr,grf->gcf', chosen, token_rows, precision=highest).reshape(groups * CAP, D)
        rows_back = jnp.einsum('gcr,grf->gcf', chosen, back_rows, precision=highest).reshape(groups * CAP, D)
        slot_prob = jnp.einsum('gcr,gr->gc', chosen, weight, precision=highest).reshape(groups * CAP)
        gate_wide = gate_weight.astype(jnp.float32)
        up_wide = up_weight.astype(jnp.float32)
        gate = jnp.dot(rows_in, gate_wide, precision=highest)
        up_part = jnp.dot(rows_in, up_wide, precision=highest)
        back_hidden = jnp.dot(rows_back, down_weight.astype(jnp.float32).T, precision=highest)
        sigmoid_gate = jax.nn.sigmoid(gate)
        active = gate * sigmoid_gate
        hidden = lax.optimization_barrier((active * up_part).astype(jnp.bfloat16)).astype(jnp.float32)
        route_part = jnp.sum(hidden * back_hidden, axis=-1).astype(jnp.bfloat16)
        scale = slot_prob[:, None]
        scaled = scale * back_hidden
        grad_g = lax.optimization_barrier((scaled * up_part * sigmoid_gate * (1.0 + gate * (1.0 - sigmoid_gate))).astype(jnp.bfloat16)).astype(jnp.float32)
        grad_u = lax.optimization_barrier((scaled * active).astype(jnp.bfloat16)).astype(jnp.float32)
        weighted = lax.optimization_barrier((scale * hidden).astype(jnp.bfloat16)).astype(jnp.float32)
        grad_down_e = jnp.dot(weighted.T, rows_back, precision=highest).astype(jnp.bfloat16)
        grad_gate_e = jnp.dot(rows_in.T, grad_g, precision=highest).astype(jnp.bfloat16)
        grad_up_e = jnp.dot(rows_in.T, grad_u, precision=highest).astype(jnp.bfloat16)
        rows_total = groups * CAP
        grad_blocks = jnp.concatenate([grad_g.reshape(rows_total, blocks, width), grad_u.reshape(rows_total, blocks, width)], axis=-1)
        weight_blocks = jnp.concatenate([gate_wide.reshape(D, blocks, width), up_wide.reshape(D, blocks, width)], axis=-1)
        pieces = jnp.einsum('rbh,dbh->rbd', grad_blocks, weight_blocks, precision=highest)
        rounded = lax.optimization_barrier(pieces.astype(jnp.bfloat16)).astype(jnp.float32)
        slot_input = jnp.sum(rounded, axis=1).astype(jnp.bfloat16).reshape(groups, CAP, D)
        return slot_input, route_part.reshape(groups, CAP), grad_gate_e, grad_up_e, grad_down_e

    slot_input, slot_route, grad_gate, grad_up, grad_down = lax.map(
        one_expert, (jnp.arange(EXPERTS, dtype=jnp.int32), w_gate, w_up, w_down))

    def table_for(expert):
        return slot_table(route_table, prob_table, expert)

    all_hits, all_weight, all_chosen = jax.vmap(table_for)(jnp.arange(EXPERTS, dtype=jnp.int32))
    input_grad = jnp.einsum('egcr,egcf->grf', all_chosen, slot_input.astype(jnp.float32), precision=highest)
    input_grad = input_grad.reshape(TOKENS, D).astype(jnp.bfloat16)
    route_grad = jnp.einsum('egcr,egrk,egc->grk', all_chosen, all_hits, slot_route.astype(jnp.float32), precision=highest)
    route_grad = route_grad.reshape(TOKENS, TOP).astype(jnp.bfloat16)
    return input_grad, route_grad, grad_gate, grad_up, grad_down
```

```python
import jax
import jax.numpy as jnp
from jax import lax
from jax.sharding import PartitionSpec as P


def advantages(row_rollout, group_ids, rewards):
    same_group = (group_ids[:, None] == group_ids[None, :]).astype(jnp.float32)
    reward_values = rewards.astype(jnp.float32)
    group_total = jnp.dot(same_group, reward_values, precision=lax.Precision.HIGHEST)
    group_count = jnp.sum(same_group, axis=1)
    per_rollout = reward_values - group_total / group_count
    member = (
        row_rollout[:, None] == jnp.arange(per_rollout.shape[0], dtype=jnp.int32)[None, :]
    ).astype(jnp.float32)
    return jnp.dot(member, per_rollout, precision=lax.Precision.HIGHEST)


def selection(routing, probs, experts, capacity):
    route_hits = (
        routing[:, :, None] == jnp.arange(experts, dtype=jnp.int32)[None, None, :]
    ).astype(jnp.float32)
    occupied = jnp.sum(route_hits, axis=1)
    weight = jnp.einsum("rke,rk->re", route_hits, probs.astype(jnp.float32))
    before = jnp.cumsum(occupied, axis=0) - occupied
    slot_index = jnp.arange(capacity, dtype=jnp.float32)
    chosen = occupied.T[:, None, :] * (before.T[:, None, :] == slot_index[None, :, None]).astype(
        jnp.float32
    )
    return (route_hits, weight, chosen)


def shards(tokens, upstream, probs, routing, row_rollout, group_ids, rewards, w_gate, w_up, w_down):
    f32 = jnp.float32
    bf16 = jnp.bfloat16
    experts = lax.axis_size("expert")
    dp_size = lax.axis_size("dp")
    tensor_size = lax.axis_size("tensor")
    group_rows, features = tokens.shape
    routes_per_row = routing.shape[1]
    capacity = min(group_rows, 5 * group_rows * routes_per_row // (4 * experts))
    slots = experts * capacity
    all_slots = dp_size * slots

    advantage = advantages(row_rollout, group_ids, rewards)
    cotangent = (advantage[:, None] * upstream.astype(f32)).astype(bf16)
    route_hits, weight, chosen = selection(routing, probs, experts, capacity)
    chosen_half = chosen.astype(bf16)

    both = jnp.stack([tokens, cotangent])
    packed = jnp.einsum(
        "ecr,arf->aecf", chosen_half, both, preferred_element_type=f32
    ).astype(bf16)
    packed_prob = jnp.einsum("ecr,re->ec", chosen, weight).astype(bf16)
    prob_row = jnp.zeros((experts, 1, features), bf16).at[:, 0, :capacity].set(packed_prob)
    prob_rows = jnp.stack([jnp.zeros_like(prob_row), prob_row])
    packed = jnp.concatenate([packed, prob_rows], axis=2)
    arrived = lax.all_to_all(packed, "expert", split_axis=1, concat_axis=1, tiled=True)
    tok_rows = arrived[0, :, :capacity].reshape(slots, features)
    cot_rows = arrived[1, :, :capacity].reshape(slots, features)
    slot_prob_local = arrived[1, :, capacity, :capacity].reshape(slots)

    g_tok = lax.all_gather(tok_rows, ("tensor", "dp"), axis=0, tiled=True)
    g_tok = g_tok.reshape(tensor_size, all_slots, features)
    g_cot = lax.all_gather(cot_rows, ("tensor", "dp"), axis=0, tiled=True)
    g_cot = g_cot.reshape(tensor_size, all_slots, features)
    slot_prob = lax.all_gather(slot_prob_local, "dp", axis=0, tiled=True)

    wg = w_gate[0].reshape(tensor_size, features, -1)
    wu = w_up[0].reshape(tensor_size, features, -1)
    wd = w_down[0]
    hidden_width = wd.shape[0]
    wd = wd.reshape(hidden_width, tensor_size, features)

    gate = sum(
        jnp.dot(g_tok[t], wg[t], preferred_element_type=f32) for t in range(tensor_size)
    )
    up_part = sum(
        jnp.dot(g_tok[t], wu[t], preferred_element_type=f32) for t in range(tensor_size)
    )
    back_hidden = sum(
        jnp.einsum("sf,hf->sh", g_cot[t], wd[:, t], preferred_element_type=f32)
        for t in range(tensor_size)
    )

    sigmoid_gate = jax.nn.sigmoid(gate)
    active = gate * sigmoid_gate
    hidden = (active * up_part).astype(bf16)
    hidden_wide = lax.optimization_barrier(hidden).astype(f32)
    route_part = jnp.sum(hidden_wide * back_hidden, axis=-1)
    scale = slot_prob.astype(f32)[:, None]
    scaled = scale * back_hidden
    grad_g = (scaled * up_part * sigmoid_gate * (1.0 + gate * (1.0 - sigmoid_gate))).astype(bf16)
    grad_u = (scaled * active).astype(bf16)
    weighted = (scale * hidden_wide).astype(bf16)

    route_total = lax.psum(route_part, ("dp", "tensor"))
    route_total, grad_g_p, grad_u_p = lax.optimization_barrier((route_total, grad_g, grad_u))

    grad_down = jnp.concatenate(
        [
            jnp.dot(weighted.T, g_cot[t], preferred_element_type=f32).astype(bf16)
            for t in range(tensor_size)
        ],
        axis=1,
    )
    grad_gate = jnp.concatenate(
        [
            jnp.dot(g_tok[t].T, grad_g, preferred_element_type=f32).astype(bf16)
            for t in range(tensor_size)
        ],
        axis=0,
    )
    grad_up = jnp.concatenate(
        [
            jnp.dot(g_tok[t].T, grad_u, preferred_element_type=f32).astype(bf16)
            for t in range(tensor_size)
        ],
        axis=0,
    )

    product = jnp.stack(
        [
            (
                jnp.einsum("sk,fk->sf", grad_g_p, wg[t], preferred_element_type=f32)
                + jnp.einsum("sk,fk->sf", grad_u_p, wu[t], preferred_element_type=f32)
            ).astype(bf16)
            for t in range(tensor_size)
        ]
    ).reshape(tensor_size * all_slots, features)
    own_rows = lax.psum_scatter(product, ("tensor", "dp"), scatter_dimension=0, tiled=True)

    own_route = lax.dynamic_slice_in_dim(
        route_total, lax.axis_index("dp") * slots, slots, 0
    ).astype(bf16)
    route_row = jnp.zeros((experts, 1, features), bf16).at[:, 0, :capacity].set(
        own_route.reshape(experts, capacity)
    )
    back_pack = jnp.concatenate([own_rows.reshape(experts, capacity, features), route_row], axis=1)
    home = lax.all_to_all(back_pack, "expert", split_axis=0, concat_axis=0, tiled=True)
    input_grad = jnp.einsum(
        "ecr,ecf->rf", chosen_half, home[:, :capacity], preferred_element_type=f32
    ).astype(bf16)
    per_expert = jnp.einsum("ecr,ec->re", chosen, home[:, capacity, :capacity].astype(f32))
    route_grad = jnp.einsum("rke,re->rk", route_hits, per_expert).astype(bf16)
    return (input_grad, route_grad, grad_gate[None], grad_up[None], grad_down[None])


def solution(mesh):
    in_specs = (
        P(("dp", "expert"), "tensor"),
        P(("dp", "expert"), "tensor"),
        P(("dp", "expert"), None),
        P(("dp", "expert"), None),
        P(("dp", "expert")),
        P(),
        P(),
        P("expert", None, ("dp", "tensor")),
        P("expert", None, ("dp", "tensor")),
        P("expert", ("dp", "tensor"), None),
    )
    out_specs = (
        P(("dp", "expert"), "tensor"),
        P(("dp", "expert"), None),
        P("expert", None, ("dp", "tensor")),
        P("expert", None, ("dp", "tensor")),
        P("expert", ("dp", "tensor"), None),
    )
    return jax.shard_map(shards, mesh=mesh, in_specs=in_specs, out_specs=out_specs, check_vma=False)
```

```python
import jax
import jax.numpy as jnp
import numpy as np
from jax import lax
from jax.sharding import Mesh
from jax.sharding import PartitionSpec as P

CORES = 2
DP = ("x", "core")


def advantages(row_rollout, group_ids, rewards):
    same_group = (group_ids[:, None] == group_ids[None, :]).astype(jnp.float32)
    reward_values = rewards.astype(jnp.float32)
    group_total = jnp.dot(same_group, reward_values, precision=lax.Precision.HIGHEST)
    group_count = jnp.sum(same_group, axis=1)
    per_rollout = reward_values - group_total / group_count
    member = (
        row_rollout[:, None] == jnp.arange(per_rollout.shape[0], dtype=jnp.int32)[None, :]
    ).astype(jnp.float32)
    return jnp.dot(member, per_rollout, precision=lax.Precision.HIGHEST)


def selection(routing, probs, experts, capacity):
    route_hits = (
        routing[:, :, None] == jnp.arange(experts, dtype=jnp.int32)[None, None, :]
    ).astype(jnp.float32)
    occupied = jnp.sum(route_hits, axis=1)
    weight = jnp.einsum("rke,rk->re", route_hits, probs.astype(jnp.float32))
    before = jnp.cumsum(occupied, axis=0) - occupied
    slot_index = jnp.arange(capacity, dtype=jnp.float32)
    chosen = occupied.T[:, None, :] * (before.T[:, None, :] == slot_index[None, :, None]).astype(
        jnp.float32
    )
    return (route_hits, weight, chosen)


def shards(tokens, upstream, probs, routing, row_rollout, group_ids, rewards, w_gate, w_up, w_down):
    f32 = jnp.float32
    bf16 = jnp.bfloat16
    experts = lax.axis_size("expert")
    n_x = lax.axis_size("x")
    n_core = lax.axis_size("core")
    n_t = lax.axis_size("tensor")
    group_rows, features = tokens.shape
    routes_per_row = routing.shape[1]
    capacity = min(group_rows, 5 * group_rows * routes_per_row // (4 * experts))
    slots = experts * capacity
    chunk = slots + 8
    per_core = n_x * chunk

    advantage = advantages(row_rollout, group_ids, rewards)
    cotangent = (advantage[:, None] * upstream.astype(f32)).astype(bf16)
    route_hits, weight, chosen = selection(routing, probs, experts, capacity)
    chosen_half = chosen.astype(bf16)

    both = jnp.stack([tokens, cotangent])
    packed = jnp.einsum(
        "ecr,arf->aecf", chosen_half, both, preferred_element_type=f32
    ).astype(bf16)
    packed_prob = jnp.einsum("ecr,re->ec", chosen, weight).astype(bf16)
    prob_row = jnp.zeros((experts, 1, features), bf16).at[:, 0, :capacity].set(packed_prob)
    prob_rows = jnp.stack([jnp.zeros_like(prob_row), prob_row])
    packed = jnp.concatenate([packed, prob_rows], axis=2)
    arrived = lax.all_to_all(packed, "expert", split_axis=1, concat_axis=1, tiled=True)
    extra = jnp.zeros((chunk - slots, features), bf16)
    extra_prob = extra.at[0, :slots].set(arrived[1, :, capacity, :capacity].reshape(slots))
    tok_rows = jnp.concatenate([arrived[0, :, :capacity].reshape(slots, features), extra_prob])
    cot_rows = jnp.concatenate([arrived[1, :, :capacity].reshape(slots, features), extra])

    def gather(rows):
        g = lax.all_gather(rows, ("tensor", "x"), axis=0, tiled=True)
        g = lax.all_gather(g, "core", axis=0, tiled=True)
        return g.reshape(n_core, n_t, per_core, features)

    g_tok = gather(tok_rows)
    g_cot = gather(cot_rows)
    slot_prob = g_tok[:, 0].reshape(n_core, n_x, chunk, features)[:, :, slots, :chunk]
    slot_prob = slot_prob.reshape(n_core * per_core)

    wg = w_gate[0].reshape(n_t, features, -1)
    wu = w_up[0].reshape(n_t, features, -1)
    wd = w_down[0]
    hidden_width = wd.shape[0]
    wd = wd.reshape(hidden_width, n_t, features)

    def over_t(fn):
        return sum(fn(t) for t in range(n_t))

    gate = jnp.concatenate(
        [
            over_t(lambda t: jnp.dot(g_tok[c, t], wg[t], preferred_element_type=f32))
            for c in range(n_core)
        ]
    )
    up_part = jnp.concatenate(
        [
            over_t(lambda t: jnp.dot(g_tok[c, t], wu[t], preferred_element_type=f32))
            for c in range(n_core)
        ]
    )
    back_hidden = jnp.concatenate(
        [
            over_t(
                lambda t: jnp.einsum(
                    "sf,hf->sh", g_cot[c, t], wd[:, t], preferred_element_type=f32
                )
            )
            for c in range(n_core)
        ]
    )

    sigmoid_gate = jax.nn.sigmoid(gate)
    active = gate * sigmoid_gate
    hidden = (active * up_part).astype(bf16)
    hidden_wide = lax.optimization_barrier(hidden).astype(f32)
    route_part = jnp.sum(hidden_wide * back_hidden, axis=-1)
    scale = slot_prob.astype(f32)[:, None]
    scaled = scale * back_hidden
    grad_g = (scaled * up_part * sigmoid_gate * (1.0 + gate * (1.0 - sigmoid_gate))).astype(bf16)
    grad_u = (scaled * active).astype(bf16)
    weighted = (scale * hidden_wide).astype(bf16)

    def rows_of(a, c):
        return a[c * per_core:(c + 1) * per_core]

    grad_down = jnp.concatenate(
        [
            sum(
                jnp.dot(rows_of(weighted, c).T, g_cot[c, t], preferred_element_type=f32)
                for c in range(n_core)
            ).astype(bf16)
            for t in range(n_t)
        ],
        axis=1,
    )
    grad_gate = jnp.concatenate(
        [
            sum(
                jnp.dot(g_tok[c, t].T, rows_of(grad_g, c), preferred_element_type=f32)
                for c in range(n_core)
            ).astype(bf16)
            for t in range(n_t)
        ],
        axis=0,
    )
    grad_up = jnp.concatenate(
        [
            sum(
                jnp.dot(g_tok[c, t].T, rows_of(grad_u, c), preferred_element_type=f32)
                for c in range(n_core)
            ).astype(bf16)
            for t in range(n_t)
        ],
        axis=0,
    )

    route_hi = route_part.astype(bf16)
    route_lo = (route_part - route_hi.astype(f32)).astype(bf16)
    route_pair = jnp.stack([route_hi, route_lo]).reshape(2, n_core, n_x, chunk)
    row_id = lax.broadcasted_iota(jnp.int32, (n_x, chunk, features), 1)
    col_id = lax.broadcasted_iota(jnp.int32, (n_x, chunk, features), 2)
    pieces = []
    for c in range(n_core):
        gc = rows_of(grad_g, c)
        uc = rows_of(grad_u, c)
        pad = jnp.zeros((n_x, chunk, features - chunk), bf16)
        hi_rows = jnp.concatenate([route_pair[0, c][:, None, :].repeat(chunk, 1), pad], axis=2)
        lo_rows = jnp.concatenate([route_pair[1, c][:, None, :].repeat(chunk, 1), pad], axis=2)
        for t in range(n_t):
            term = (
                jnp.einsum("sk,fk->sf", gc, wg[t], preferred_element_type=f32)
                + jnp.einsum("sk,fk->sf", uc, wu[t], preferred_element_type=f32)
            ).astype(bf16).reshape(n_x, chunk, features)
            term = jnp.where(row_id == slots, hi_rows, term)
            term = jnp.where(row_id == slots + 1, lo_rows, term)
            pieces.append(term)
    product = jnp.stack(pieces).reshape(n_core * n_t * per_core, features)
    summed = lax.psum_scatter(product, "core", scatter_dimension=0, tiled=True)
    own_rows = lax.psum_scatter(summed, ("tensor", "x"), scatter_dimension=0, tiled=True)

    own_route = (
        own_rows[slots, :slots].astype(f32) + own_rows[slots + 1, :slots].astype(f32)
    ).astype(bf16)
    route_row = jnp.zeros((experts, 1, features), bf16).at[:, 0, :capacity].set(
        own_route.reshape(experts, capacity)
    )
    back_pack = jnp.concatenate(
        [own_rows[:slots].reshape(experts, capacity, features), route_row], axis=1
    )
    home = lax.all_to_all(back_pack, "expert", split_axis=0, concat_axis=0, tiled=True)
    input_grad = jnp.einsum(
        "ecr,ecf->rf", chosen_half, home[:, :capacity], preferred_element_type=f32
    ).astype(bf16)
    per_expert = jnp.einsum("ecr,ec->re", chosen, home[:, capacity, :capacity].astype(f32))
    route_grad = jnp.einsum("rke,re->rk", route_hits, per_expert).astype(bf16)
    return (input_grad, route_grad, grad_gate[None], grad_up[None], grad_down[None])


def solution(mesh):
    n_dp = mesh.shape["dp"]
    devices = np.asarray(mesh.devices).reshape(
        n_dp // CORES, CORES, mesh.shape["expert"], mesh.shape["tensor"]
    )
    split_mesh = Mesh(devices, ("x", "core", "expert", "tensor"))
    rows = DP + ("expert",)
    in_specs = (
        P(rows, "tensor"),
        P(rows, "tensor"),
        P(rows, None),
        P(rows, None),
        P(rows),
        P(),
        P(),
        P("expert", None, DP + ("tensor",)),
        P("expert", None, DP + ("tensor",)),
        P("expert", DP + ("tensor",), None),
    )
    out_specs = (
        P(rows, "tensor"),
        P(rows, None),
        P("expert", None, DP + ("tensor",)),
        P("expert", None, DP + ("tensor",)),
        P("expert", DP + ("tensor",), None),
    )
    return jax.shard_map(
        shards, mesh=split_mesh, in_specs=in_specs, out_specs=out_specs, check_vma=False
    )
```

```python
import jax
import jax.numpy as jnp
from jax import lax
from jax.sharding import PartitionSpec as P


def advantages(row_rollout, group_ids, rewards):
    same_group = (group_ids[:, None] == group_ids[None, :]).astype(jnp.float32)
    reward_values = rewards.astype(jnp.float32)
    group_total = jnp.dot(same_group, reward_values, precision=lax.Precision.HIGHEST)
    group_count = jnp.sum(same_group, axis=1)
    per_rollout = reward_values - group_total / group_count
    member = (
        row_rollout[:, None] == jnp.arange(per_rollout.shape[0], dtype=jnp.int32)[None, :]
    ).astype(jnp.float32)
    return jnp.dot(member, per_rollout, precision=lax.Precision.HIGHEST)


def selection(routing, probs, experts, capacity):
    route_hits = (
        routing[:, :, None] == jnp.arange(experts, dtype=jnp.int32)[None, None, :]
    ).astype(jnp.float32)
    occupied = jnp.sum(route_hits, axis=1)
    weight = jnp.einsum("rke,rk->re", route_hits, probs.astype(jnp.float32))
    before = jnp.cumsum(occupied, axis=0) - occupied
    slot_index = jnp.arange(capacity, dtype=jnp.float32)
    chosen = occupied.T[:, None, :] * (before.T[:, None, :] == slot_index[None, :, None]).astype(
        jnp.float32
    )
    return (route_hits, weight, chosen)


def shards(tokens, upstream, probs, routing, row_rollout, group_ids, rewards, w_gate, w_up, w_down):
    f32 = jnp.float32
    bf16 = jnp.bfloat16
    experts = lax.axis_size("expert")
    dp_size = lax.axis_size("dp")
    tensor_size = lax.axis_size("tensor")
    group_rows, features = tokens.shape
    routes_per_row = routing.shape[1]
    capacity = min(group_rows, 5 * group_rows * routes_per_row // (4 * experts))
    slots = experts * capacity

    advantage = advantages(row_rollout, group_ids, rewards)
    cotangent = (advantage[:, None] * upstream.astype(f32)).astype(bf16)
    route_hits, weight, chosen = selection(routing, probs, experts, capacity)
    chosen_half = chosen.astype(bf16)

    both = jnp.stack([tokens, cotangent])
    packed = jnp.einsum(
        "ecr,arf->aecf", chosen_half, both, preferred_element_type=f32
    ).astype(bf16)
    packed_prob = jnp.einsum("ecr,re->ec", chosen, weight).astype(bf16)
    prob_row = jnp.zeros((experts, 1, features), bf16).at[:, 0, :capacity].set(packed_prob)
    prob_rows = jnp.stack([jnp.zeros_like(prob_row), prob_row])
    packed = jnp.concatenate([packed, prob_rows], axis=2)
    arrived = lax.all_to_all(packed, "expert", split_axis=1, concat_axis=1, tiled=True)
    chunk = slots + 8
    all_rows = dp_size * chunk
    extra = jnp.zeros((chunk - slots, features), bf16)
    extra_prob = extra.at[0, :slots].set(arrived[1, :, capacity, :capacity].reshape(slots))
    tok_rows = jnp.concatenate([arrived[0, :, :capacity].reshape(slots, features), extra_prob])
    cot_rows = jnp.concatenate([arrived[1, :, :capacity].reshape(slots, features), extra])

    g_tok = lax.all_gather(tok_rows, ("tensor", "dp"), axis=0, tiled=True)
    g_tok = g_tok.reshape(tensor_size, all_rows, features)
    g_cot = lax.all_gather(cot_rows, ("tensor", "dp"), axis=0, tiled=True)
    g_cot = g_cot.reshape(tensor_size, all_rows, features)
    slot_prob = g_tok[0].reshape(dp_size, chunk, features)[:, slots, :chunk].reshape(all_rows)

    wg = w_gate[0].reshape(tensor_size, features, -1)
    wu = w_up[0].reshape(tensor_size, features, -1)
    wd = w_down[0]
    hidden_width = wd.shape[0]
    wd = wd.reshape(hidden_width, tensor_size, features)

    w_in = jnp.concatenate([wg, wu], axis=2)
    gate_up = sum(
        jnp.dot(g_tok[t], w_in[t], preferred_element_type=f32) for t in range(tensor_size)
    )
    gate = gate_up[:, :hidden_width]
    up_part = gate_up[:, hidden_width:]
    back_hidden = sum(
        jnp.einsum("sf,hf->sh", g_cot[t], wd[:, t], preferred_element_type=f32)
        for t in range(tensor_size)
    )

    sigmoid_gate = jax.nn.sigmoid(gate)
    active = gate * sigmoid_gate
    hidden = (active * up_part).astype(bf16)
    hidden_wide = lax.optimization_barrier(hidden).astype(f32)
    route_part = jnp.sum(hidden_wide * back_hidden, axis=-1)
    scale = slot_prob.astype(f32)[:, None]
    scaled = scale * back_hidden
    grad_g = (scaled * up_part * sigmoid_gate * (1.0 + gate * (1.0 - sigmoid_gate))).astype(bf16)
    grad_u = (scaled * active).astype(bf16)
    weighted = (scale * hidden_wide).astype(bf16)

    grad_down = jnp.concatenate(
        [
            jnp.dot(weighted.T, g_cot[t], preferred_element_type=f32).astype(bf16)
            for t in range(tensor_size)
        ],
        axis=1,
    )
    grad_gate = jnp.concatenate(
        [
            jnp.dot(g_tok[t].T, grad_g, preferred_element_type=f32).astype(bf16)
            for t in range(tensor_size)
        ],
        axis=0,
    )
    grad_up = jnp.concatenate(
        [
            jnp.dot(g_tok[t].T, grad_u, preferred_element_type=f32).astype(bf16)
            for t in range(tensor_size)
        ],
        axis=0,
    )

    route_hi = route_part.astype(bf16).reshape(dp_size, chunk)
    route_lo = (route_part.reshape(dp_size, chunk) - route_hi.astype(f32)).astype(bf16)
    carry = jnp.zeros((dp_size, chunk, hidden_width), bf16)
    carry = carry.at[:, slots, :chunk].set(route_hi).at[:, slots + 1, :chunk].set(route_lo)
    lhs = jnp.concatenate([grad_g, grad_u, carry.reshape(all_rows, hidden_width)], axis=1)
    eye = (
        lax.broadcasted_iota(jnp.int32, (features, hidden_width), 0)
        == lax.broadcasted_iota(jnp.int32, (features, hidden_width), 1)
    ).astype(bf16)
    w_out = jnp.concatenate([wg, wu, jnp.broadcast_to(eye, wg.shape)], axis=2)
    product = jnp.stack(
        [
            jnp.einsum("sk,fk->sf", lhs, w_out[t], preferred_element_type=f32).astype(bf16)
            for t in range(tensor_size)
        ]
    ).reshape(tensor_size * all_rows, features)
    own_rows = lax.psum_scatter(product, ("tensor", "dp"), scatter_dimension=0, tiled=True)

    own_route = (
        own_rows[slots, :slots].astype(f32) + own_rows[slots + 1, :slots].astype(f32)
    ).astype(bf16)
    partner = lax.ppermute(own_route, "tensor", [(i, i ^ 1) for i in range(tensor_size)])
    own_route = jnp.where(lax.axis_index("tensor") == 0, own_route, partner)
    route_row = jnp.zeros((experts, 1, features), bf16).at[:, 0, :capacity].set(
        own_route.reshape(experts, capacity)
    )
    back_pack = jnp.concatenate(
        [own_rows[:slots].reshape(experts, capacity, features), route_row], axis=1
    )
    home = lax.all_to_all(back_pack, "expert", split_axis=0, concat_axis=0, tiled=True)
    input_grad = jnp.einsum(
        "ecr,ecf->rf", chosen_half, home[:, :capacity], preferred_element_type=f32
    ).astype(bf16)
    per_expert = jnp.einsum("ecr,ec->re", chosen, home[:, capacity, :capacity].astype(f32))
    route_grad = jnp.einsum("rke,re->rk", route_hits, per_expert).astype(bf16)
    return (input_grad, route_grad, grad_gate[None], grad_up[None], grad_down[None])


def solution(mesh):
    in_specs = (
        P(("dp", "expert"), "tensor"),
        P(("dp", "expert"), "tensor"),
        P(("dp", "expert"), None),
        P(("dp", "expert"), None),
        P(("dp", "expert")),
        P(),
        P(),
        P("expert", None, ("dp", "tensor")),
        P("expert", None, ("dp", "tensor")),
        P("expert", ("dp", "tensor"), None),
    )
    out_specs = (
        P(("dp", "expert"), "tensor"),
        P(("dp", "expert"), None),
        P("expert", None, ("dp", "tensor")),
        P("expert", None, ("dp", "tensor")),
        P("expert", ("dp", "tensor"), None),
    )
    return jax.shard_map(shards, mesh=mesh, in_specs=in_specs, out_specs=out_specs, check_vma=False)
```

```python
import jax
import jax.numpy as jnp
from jax import lax
from jax.sharding import PartitionSpec as P


def advantages(row_rollout, group_ids, rewards):
    same_group = (group_ids[:, None] == group_ids[None, :]).astype(jnp.float32)
    reward_values = rewards.astype(jnp.float32)
    group_total = jnp.dot(same_group, reward_values, precision=lax.Precision.HIGHEST)
    group_count = jnp.sum(same_group, axis=1)
    per_rollout = reward_values - group_total / group_count
    member = (
        row_rollout[:, None] == jnp.arange(per_rollout.shape[0], dtype=jnp.int32)[None, :]
    ).astype(jnp.float32)
    return jnp.dot(member, per_rollout, precision=lax.Precision.HIGHEST)


def selection(routing, probs, experts, capacity):
    route_hits = (
        routing[:, :, None] == jnp.arange(experts, dtype=jnp.int32)[None, None, :]
    ).astype(jnp.float32)
    occupied = jnp.sum(route_hits, axis=1)
    weight = jnp.einsum("rke,rk->re", route_hits, probs.astype(jnp.float32))
    before = jnp.cumsum(occupied, axis=0) - occupied
    slot_index = jnp.arange(capacity, dtype=jnp.float32)
    chosen = occupied.T[:, None, :] * (before.T[:, None, :] == slot_index[None, :, None]).astype(
        jnp.float32
    )
    return (route_hits, weight, chosen)


def shards(tokens, upstream, probs, routing, row_rollout, group_ids, rewards, w_gate, w_up, w_down):
    f32 = jnp.float32
    bf16 = jnp.bfloat16
    experts = lax.axis_size("expert")
    dp_size = lax.axis_size("dp")
    tensor_size = lax.axis_size("tensor")
    group_rows, features = tokens.shape
    routes_per_row = routing.shape[1]
    capacity = min(group_rows, 5 * group_rows * routes_per_row // (4 * experts))
    slots = experts * capacity

    advantage = advantages(row_rollout, group_ids, rewards)
    cotangent = (advantage[:, None] * upstream.astype(f32)).astype(bf16)
    route_hits, weight, chosen = selection(routing, probs, experts, capacity)
    me = lax.axis_index("expert")
    shifted = (me + jnp.arange(experts, dtype=jnp.int32)) % experts
    chosen = jnp.take(chosen, shifted, axis=0)
    chosen_half = chosen.astype(bf16)
    weight = jnp.take(weight, shifted, axis=1)
    route_hits = jnp.take(route_hits, shifted, axis=2)

    both = jnp.stack([tokens, cotangent])
    packed = jnp.einsum(
        "ecr,arf->aecf", chosen_half, both, preferred_element_type=f32
    ).astype(bf16)
    packed_prob = jnp.einsum("ecr,re->ec", chosen, weight).astype(bf16)
    prob_row = jnp.zeros((experts, 1, features), bf16).at[:, 0, :capacity].set(packed_prob)
    prob_rows = jnp.stack([jnp.zeros_like(prob_row), prob_row])
    packed = jnp.concatenate([packed, prob_rows], axis=2)

    def shift_ring(blocks, sign):
        out = [blocks[0]]
        for k in range(1, experts):
            perm = [(i, (i + sign * k) % experts) for i in range(experts)]
            out.append(lax.ppermute(blocks[k], "expert", perm))
        return jnp.stack(out)

    arrived = shift_ring([packed[:, k] for k in range(experts)], 1).transpose(1, 0, 2, 3)
    chunk = slots + 8
    all_rows = dp_size * chunk
    extra = jnp.zeros((chunk - slots, features), bf16)
    extra_prob = extra.at[0, :slots].set(arrived[1, :, capacity, :capacity].reshape(slots))
    tok_rows = jnp.concatenate([arrived[0, :, :capacity].reshape(slots, features), extra_prob])
    cot_rows = jnp.concatenate([arrived[1, :, :capacity].reshape(slots, features), extra])

    g_tok = lax.all_gather(tok_rows, ("tensor", "dp"), axis=0, tiled=True)
    g_tok = g_tok.reshape(tensor_size, all_rows, features)
    g_cot = lax.all_gather(cot_rows, ("tensor", "dp"), axis=0, tiled=True)
    g_cot = g_cot.reshape(tensor_size, all_rows, features)
    slot_prob = g_tok[0].reshape(dp_size, chunk, features)[:, slots, :chunk].reshape(all_rows)

    wg = w_gate[0].reshape(tensor_size, features, -1)
    wu = w_up[0].reshape(tensor_size, features, -1)
    wd = w_down[0]
    hidden_width = wd.shape[0]
    wd = wd.reshape(hidden_width, tensor_size, features)

    w_in = jnp.concatenate([wg, wu], axis=2)
    gate_up = sum(
        jnp.dot(g_tok[t], w_in[t], preferred_element_type=f32) for t in range(tensor_size)
    )
    gate = gate_up[:, :hidden_width]
    up_part = gate_up[:, hidden_width:]
    back_hidden = sum(
        jnp.einsum("sf,hf->sh", g_cot[t], wd[:, t], preferred_element_type=f32)
        for t in range(tensor_size)
    )

    sigmoid_gate = jax.nn.sigmoid(gate)
    active = gate * sigmoid_gate
    hidden = (active * up_part).astype(bf16)
    hidden_wide = lax.optimization_barrier(hidden).astype(f32)
    route_part = jnp.sum(hidden_wide * back_hidden, axis=-1)
    scale = slot_prob.astype(f32)[:, None]
    scaled = scale * back_hidden
    grad_g = (scaled * up_part * sigmoid_gate * (1.0 + gate * (1.0 - sigmoid_gate))).astype(bf16)
    grad_u = (scaled * active).astype(bf16)
    weighted = (scale * hidden_wide).astype(bf16)

    grad_down = jnp.concatenate(
        [
            jnp.dot(weighted.T, g_cot[t], preferred_element_type=f32).astype(bf16)
            for t in range(tensor_size)
        ],
        axis=1,
    )
    grad_gate = jnp.concatenate(
        [
            jnp.dot(g_tok[t].T, grad_g, preferred_element_type=f32).astype(bf16)
            for t in range(tensor_size)
        ],
        axis=0,
    )
    grad_up = jnp.concatenate(
        [
            jnp.dot(g_tok[t].T, grad_u, preferred_element_type=f32).astype(bf16)
            for t in range(tensor_size)
        ],
        axis=0,
    )

    route_hi = route_part.astype(bf16).reshape(dp_size, chunk)
    route_lo = (route_part.reshape(dp_size, chunk) - route_hi.astype(f32)).astype(bf16)
    carry = jnp.zeros((dp_size, chunk, hidden_width), bf16)
    carry = carry.at[:, slots, :chunk].set(route_hi).at[:, slots + 1, :chunk].set(route_lo)
    lhs = jnp.concatenate([grad_g, grad_u, carry.reshape(all_rows, hidden_width)], axis=1)
    eye = (
        lax.broadcasted_iota(jnp.int32, (features, hidden_width), 0)
        == lax.broadcasted_iota(jnp.int32, (features, hidden_width), 1)
    ).astype(bf16)
    w_out = jnp.concatenate([wg, wu, jnp.broadcast_to(eye, wg.shape)], axis=2)
    product = jnp.stack(
        [
            jnp.einsum("sk,fk->sf", lhs, w_out[t], preferred_element_type=f32).astype(bf16)
            for t in range(tensor_size)
        ]
    ).reshape(tensor_size * all_rows, features)
    own_rows = lax.psum_scatter(product, ("tensor", "dp"), scatter_dimension=0, tiled=True)

    own_route = (
        own_rows[slots, :slots].astype(f32) + own_rows[slots + 1, :slots].astype(f32)
    ).astype(bf16)
    partner = lax.ppermute(own_route, "tensor", [(i, i ^ 1) for i in range(tensor_size)])
    own_route = jnp.where(lax.axis_index("tensor") == 0, own_route, partner)
    route_row = jnp.zeros((experts, 1, features), bf16).at[:, 0, :capacity].set(
        own_route.reshape(experts, capacity)
    )
    back_pack = jnp.concatenate(
        [own_rows[:slots].reshape(experts, capacity, features), route_row], axis=1
    )
    home = shift_ring([back_pack[k] for k in range(experts)], -1)
    input_grad = jnp.einsum(
        "ecr,ecf->rf", chosen_half, home[:, :capacity], preferred_element_type=f32
    ).astype(bf16)
    per_expert = jnp.einsum("ecr,ec->re", chosen, home[:, capacity, :capacity].astype(f32))
    route_grad = jnp.einsum("rke,re->rk", route_hits, per_expert).astype(bf16)
    return (input_grad, route_grad, grad_gate[None], grad_up[None], grad_down[None])


def solution(mesh):
    in_specs = (
        P(("dp", "expert"), "tensor"),
        P(("dp", "expert"), "tensor"),
        P(("dp", "expert"), None),
        P(("dp", "expert"), None),
        P(("dp", "expert")),
        P(),
        P(),
        P("expert", None, ("dp", "tensor")),
        P("expert", None, ("dp", "tensor")),
        P("expert", ("dp", "tensor"), None),
    )
    out_specs = (
        P(("dp", "expert"), "tensor"),
        P(("dp", "expert"), None),
        P("expert", None, ("dp", "tensor")),
        P("expert", None, ("dp", "tensor")),
        P("expert", ("dp", "tensor"), None),
    )
    return jax.shard_map(shards, mesh=mesh, in_specs=in_specs, out_specs=out_specs, check_vma=False)
```

```python
import jax
import jax.numpy as jnp
from jax import lax
from jax.sharding import PartitionSpec as P


def advantages(row_rollout, group_ids, rewards):
    same_group = (group_ids[:, None] == group_ids[None, :]).astype(jnp.float32)
    reward_values = rewards.astype(jnp.float32)
    group_total = jnp.dot(same_group, reward_values, precision=lax.Precision.HIGHEST)
    group_count = jnp.sum(same_group, axis=1)
    per_rollout = reward_values - group_total / group_count
    member = (
        row_rollout[:, None] == jnp.arange(per_rollout.shape[0], dtype=jnp.int32)[None, :]
    ).astype(jnp.float32)
    return jnp.dot(member, per_rollout, precision=lax.Precision.HIGHEST)


def selection(routing, probs, experts, capacity):
    route_hits = (
        routing[:, :, None] == jnp.arange(experts, dtype=jnp.int32)[None, None, :]
    ).astype(jnp.float32)
    occupied = jnp.sum(route_hits, axis=1)
    weight = jnp.einsum("rke,rk->re", route_hits, probs.astype(jnp.float32))
    before = jnp.cumsum(occupied, axis=0) - occupied
    slot_index = jnp.arange(capacity, dtype=jnp.float32)
    chosen = occupied.T[:, None, :] * (before.T[:, None, :] == slot_index[None, :, None]).astype(
        jnp.float32
    )
    return (route_hits, weight, chosen)


def shards(tokens, upstream, probs, routing, row_rollout, group_ids, rewards, w_gate, w_up, w_down):
    f32 = jnp.float32
    bf16 = jnp.bfloat16
    experts = lax.axis_size("expert")
    dp_size = lax.axis_size("dp")
    tensor_size = lax.axis_size("tensor")
    group_rows, features = tokens.shape
    routes_per_row = routing.shape[1]
    capacity = min(group_rows, 5 * group_rows * routes_per_row // (4 * experts))
    slots = experts * capacity

    advantage = advantages(row_rollout, group_ids, rewards)
    cotangent = (advantage[:, None] * upstream.astype(f32)).astype(bf16)
    route_hits, weight, chosen = selection(routing, probs, experts, capacity)
    chosen_half = chosen.astype(bf16)

    both = jnp.stack([tokens, cotangent])
    packed = jnp.einsum(
        "ecr,arf->aecf", chosen_half, both, preferred_element_type=f32
    ).astype(bf16)
    packed_prob = jnp.einsum("ecr,re->ec", chosen, weight).astype(bf16)
    prob_row = jnp.zeros((experts, 1, features), bf16).at[:, 0, :capacity].set(packed_prob)
    prob_rows = jnp.stack([jnp.zeros_like(prob_row), prob_row])
    packed = jnp.concatenate([packed, prob_rows], axis=2)
    arrived = lax.all_to_all(packed, "expert", split_axis=1, concat_axis=1, tiled=True)
    chunk = slots + 8
    all_rows = dp_size * chunk
    extra = jnp.zeros((chunk - slots, features), bf16)
    extra_prob = extra.at[0, :slots].set(arrived[1, :, capacity, :capacity].reshape(slots))
    tok_rows = jnp.concatenate([arrived[0, :, :capacity].reshape(slots, features), extra_prob])
    cot_rows = jnp.concatenate([arrived[1, :, :capacity].reshape(slots, features), extra])

    g_tok = lax.all_gather(tok_rows, ("tensor", "dp"), axis=0, tiled=True)
    g_tok = g_tok.reshape(tensor_size, all_rows, features)
    g_cot = lax.all_gather(cot_rows, ("tensor", "dp"), axis=0, tiled=True)
    g_cot = g_cot.reshape(tensor_size, all_rows, features)
    slot_prob = g_tok[0].reshape(dp_size, chunk, features)[:, slots, :chunk].reshape(all_rows)

    wg = w_gate[0].reshape(tensor_size, features, -1)
    wu = w_up[0].reshape(tensor_size, features, -1)
    wd = w_down[0]
    hidden_width = wd.shape[0]
    wd = wd.reshape(hidden_width, tensor_size, features)

    w_in = jnp.concatenate([wg, wu], axis=2)
    gate_up = sum(
        jnp.dot(g_tok[t], w_in[t], preferred_element_type=f32) for t in range(tensor_size)
    )
    gate = gate_up[:, :hidden_width]
    up_part = gate_up[:, hidden_width:]
    back_hidden = sum(
        jnp.einsum("sf,hf->sh", g_cot[t], wd[:, t], preferred_element_type=f32)
        for t in range(tensor_size)
    )

    sigmoid_gate = jax.nn.sigmoid(gate)
    active = gate * sigmoid_gate
    hidden = (active * up_part).astype(bf16)
    hidden_wide = lax.optimization_barrier(hidden).astype(f32)
    route_part = jnp.sum(hidden_wide * back_hidden, axis=-1)
    scale = slot_prob.astype(f32)[:, None]
    scaled = scale * back_hidden
    grad_g = (scaled * up_part * sigmoid_gate * (1.0 + gate * (1.0 - sigmoid_gate))).astype(bf16)
    grad_u = (scaled * active).astype(bf16)
    weighted = (scale * hidden_wide).astype(bf16)

    grad_down = jnp.concatenate(
        [
            jnp.dot(weighted.T, g_cot[t], preferred_element_type=f32).astype(bf16)
            for t in range(tensor_size)
        ],
        axis=1,
    )
    grad_gate = jnp.concatenate(
        [
            jnp.dot(g_tok[t].T, grad_g, preferred_element_type=f32).astype(bf16)
            for t in range(tensor_size)
        ],
        axis=0,
    )
    grad_up = jnp.concatenate(
        [
            jnp.dot(g_tok[t].T, grad_u, preferred_element_type=f32).astype(bf16)
            for t in range(tensor_size)
        ],
        axis=0,
    )

    route_hi = route_part.astype(bf16).reshape(dp_size, chunk)
    route_lo = (route_part.reshape(dp_size, chunk) - route_hi.astype(f32)).astype(bf16)
    carry = jnp.zeros((dp_size, chunk, hidden_width), bf16)
    carry = carry.at[:, slots, :chunk].set(route_hi).at[:, slots + 1, :chunk].set(route_lo)
    lhs = jnp.concatenate([grad_g, grad_u, carry.reshape(all_rows, hidden_width)], axis=1)
    eye = (
        lax.broadcasted_iota(jnp.int32, (features, hidden_width), 0)
        == lax.broadcasted_iota(jnp.int32, (features, hidden_width), 1)
    ).astype(bf16)
    w_out = jnp.concatenate([wg, wu, jnp.broadcast_to(eye, wg.shape)], axis=2)
    product = jnp.einsum("sk,tfk->tsf", lhs, w_out, preferred_element_type=f32).astype(bf16)
    product = product.reshape(tensor_size * all_rows, features)
    own_rows = lax.psum_scatter(product, ("tensor", "dp"), scatter_dimension=0, tiled=True)

    own_route = (
        own_rows[slots, :slots].astype(f32) + own_rows[slots + 1, :slots].astype(f32)
    ).astype(bf16)
    partner = lax.ppermute(own_route, "tensor", [(i, i ^ 1) for i in range(tensor_size)])
    own_route = jnp.where(lax.axis_index("tensor") == 0, own_route, partner)
    route_row = jnp.zeros((experts, 1, features), bf16).at[:, 0, :capacity].set(
        own_route.reshape(experts, capacity)
    )
    back_pack = jnp.concatenate(
        [own_rows[:slots].reshape(experts, capacity, features), route_row], axis=1
    )
    home = lax.all_to_all(back_pack, "expert", split_axis=0, concat_axis=0, tiled=True)
    input_grad = jnp.einsum(
        "ecr,ecf->rf", chosen_half, home[:, :capacity], preferred_element_type=f32
    ).astype(bf16)
    per_expert = jnp.einsum("ecr,ec->re", chosen, home[:, capacity, :capacity].astype(f32))
    route_grad = jnp.einsum("rke,re->rk", route_hits, per_expert).astype(bf16)
    return (input_grad, route_grad, grad_gate[None], grad_up[None], grad_down[None])


def solution(mesh):
    in_specs = (
        P(("dp", "expert"), "tensor"),
        P(("dp", "expert"), "tensor"),
        P(("dp", "expert"), None),
        P(("dp", "expert"), None),
        P(("dp", "expert")),
        P(),
        P(),
        P("expert", None, ("dp", "tensor")),
        P("expert", None, ("dp", "tensor")),
        P("expert", ("dp", "tensor"), None),
    )
    out_specs = (
        P(("dp", "expert"), "tensor"),
        P(("dp", "expert"), None),
        P("expert", None, ("dp", "tensor")),
        P("expert", None, ("dp", "tensor")),
        P("expert", ("dp", "tensor"), None),
    )
    return jax.shard_map(shards, mesh=mesh, in_specs=in_specs, out_specs=out_specs, check_vma=False)
```

```python
import jax
import jax.numpy as jnp
from jax import lax
from jax.sharding import PartitionSpec as P


def advantages(row_rollout, group_ids, rewards):
    same_group = (group_ids[:, None] == group_ids[None, :]).astype(jnp.float32)
    reward_values = rewards.astype(jnp.float32)
    group_total = jnp.dot(same_group, reward_values, precision=lax.Precision.HIGHEST)
    group_count = jnp.sum(same_group, axis=1)
    per_rollout = reward_values - group_total / group_count
    member = (
        row_rollout[:, None] == jnp.arange(per_rollout.shape[0], dtype=jnp.int32)[None, :]
    ).astype(jnp.float32)
    return jnp.dot(member, per_rollout, precision=lax.Precision.HIGHEST)


def selection(routing, probs, experts, capacity):
    route_hits = (
        routing[:, :, None] == jnp.arange(experts, dtype=jnp.int32)[None, None, :]
    ).astype(jnp.float32)
    occupied = jnp.sum(route_hits, axis=1)
    weight = jnp.einsum("rke,rk->re", route_hits, probs.astype(jnp.float32))
    before = jnp.cumsum(occupied, axis=0) - occupied
    slot_index = jnp.arange(capacity, dtype=jnp.float32)
    chosen = occupied.T[:, None, :] * (before.T[:, None, :] == slot_index[None, :, None]).astype(
        jnp.float32
    )
    return (route_hits, weight, chosen)


def shards(tokens, upstream, probs, routing, row_rollout, group_ids, rewards, w_gate, w_up, w_down):
    f32 = jnp.float32
    bf16 = jnp.bfloat16
    experts = lax.axis_size("expert")
    dp_size = lax.axis_size("dp")
    tensor_size = lax.axis_size("tensor")
    group_rows, features = tokens.shape
    routes_per_row = routing.shape[1]
    capacity = min(group_rows, 5 * group_rows * routes_per_row // (4 * experts))
    slots = experts * capacity

    advantage = advantages(row_rollout, group_ids, rewards)
    cotangent = (advantage[:, None] * upstream.astype(f32)).astype(bf16)
    route_hits, weight, chosen = selection(routing, probs, experts, capacity)
    chosen_half = chosen.astype(bf16)

    both = jnp.stack([tokens, cotangent])
    packed = jnp.einsum(
        "ecr,arf->aecf", chosen_half, both, preferred_element_type=f32
    ).astype(bf16)
    packed_prob = jnp.einsum("ecr,re->ec", chosen, weight).astype(bf16)
    prob_row = jnp.zeros((experts, 1, features), bf16).at[:, 0, :capacity].set(packed_prob)
    prob_rows = jnp.stack([jnp.zeros_like(prob_row), prob_row])
    packed = jnp.concatenate([packed, prob_rows], axis=2)
    arrived = lax.all_to_all(packed, "expert", split_axis=1, concat_axis=1, tiled=True)
    chunk = slots + 8
    all_rows = dp_size * chunk
    extra = jnp.zeros((chunk - slots, features), bf16)
    extra_prob = extra.at[0, :slots].set(arrived[1, :, capacity, :capacity].reshape(slots))
    tok_rows = jnp.concatenate([arrived[0, :, :capacity].reshape(slots, features), extra_prob])
    cot_rows = jnp.concatenate([arrived[1, :, :capacity].reshape(slots, features), extra])

    g_tok = lax.all_gather(tok_rows, ("tensor", "dp"), axis=0, tiled=True)
    g_tok = g_tok.reshape(tensor_size, all_rows, features)
    g_cot = lax.all_gather(cot_rows, ("tensor", "dp"), axis=0, tiled=True)
    g_cot = g_cot.reshape(tensor_size, all_rows, features)
    slot_prob = g_tok[0].reshape(dp_size, chunk, features)[:, slots, :chunk].reshape(all_rows)

    wg = w_gate[0].reshape(tensor_size, features, -1)
    wu = w_up[0].reshape(tensor_size, features, -1)
    wd = w_down[0]
    hidden_width = wd.shape[0]
    wd = wd.reshape(hidden_width, tensor_size, features)

    w_in = jnp.concatenate([wg, wu], axis=2)
    gate_up = sum(
        jnp.dot(g_tok[t], w_in[t], preferred_element_type=f32) for t in range(tensor_size)
    )
    gate = gate_up[:, :hidden_width]
    up_part = gate_up[:, hidden_width:]
    back_hidden = sum(
        jnp.einsum("sf,hf->sh", g_cot[t], wd[:, t], preferred_element_type=f32)
        for t in range(tensor_size)
    )

    sigmoid_gate = jax.nn.sigmoid(gate)
    active = gate * sigmoid_gate
    hidden = (active * up_part).astype(bf16)
    hidden_wide = lax.optimization_barrier(hidden).astype(f32)
    route_part = jnp.sum(hidden_wide * back_hidden, axis=-1)
    scale = slot_prob.astype(f32)[:, None]
    scaled = scale * back_hidden
    grad_g = (scaled * up_part * sigmoid_gate * (1.0 + gate * (1.0 - sigmoid_gate))).astype(bf16)
    grad_u = (scaled * active).astype(bf16)
    weighted = (scale * hidden_wide).astype(bf16)

    grad_down = jnp.concatenate(
        [
            jnp.dot(weighted.T, g_cot[t], preferred_element_type=f32).astype(bf16)
            for t in range(tensor_size)
        ],
        axis=1,
    )
    grad_gate = jnp.concatenate(
        [
            jnp.dot(g_tok[t].T, grad_g, preferred_element_type=f32).astype(bf16)
            for t in range(tensor_size)
        ],
        axis=0,
    )
    grad_up = jnp.concatenate(
        [
            jnp.dot(g_tok[t].T, grad_u, preferred_element_type=f32).astype(bf16)
            for t in range(tensor_size)
        ],
        axis=0,
    )

    route_hi = route_part.astype(bf16).reshape(dp_size, chunk)
    route_lo = (route_part.reshape(dp_size, chunk) - route_hi.astype(f32)).astype(bf16)
    carry = jnp.zeros((dp_size, chunk, hidden_width), bf16)
    carry = carry.at[:, slots, :chunk].set(route_hi).at[:, slots + 1, :chunk].set(route_lo)
    lhs = jnp.concatenate([grad_g, grad_u, carry.reshape(all_rows, hidden_width)], axis=1)
    eye = (
        lax.broadcasted_iota(jnp.int32, (features, hidden_width), 0)
        == lax.broadcasted_iota(jnp.int32, (features, hidden_width), 1)
    ).astype(bf16)
    w_out = jnp.concatenate([wg, wu, jnp.broadcast_to(eye, wg.shape)], axis=2)
    product = jnp.einsum("sk,tfk->tsf", lhs, w_out, preferred_element_type=f32).astype(bf16)
    product = product.reshape(tensor_size * all_rows, features)
    own_rows = lax.psum_scatter(product, ("tensor", "dp"), scatter_dimension=0, tiled=True)
    own_rows, grad_gate, grad_up, grad_down = lax.optimization_barrier(
        (own_rows, grad_gate, grad_up, grad_down)
    )

    own_route = (
        own_rows[slots, :slots].astype(f32) + own_rows[slots + 1, :slots].astype(f32)
    ).astype(bf16)
    partner = lax.ppermute(own_route, "tensor", [(i, i ^ 1) for i in range(tensor_size)])
    own_route = jnp.where(lax.axis_index("tensor") == 0, own_route, partner)
    route_row = jnp.zeros((experts, 1, features), bf16).at[:, 0, :capacity].set(
        own_route.reshape(experts, capacity)
    )
    back_pack = jnp.concatenate(
        [own_rows[:slots].reshape(experts, capacity, features), route_row], axis=1
    )
    home = lax.all_to_all(back_pack, "expert", split_axis=0, concat_axis=0, tiled=True)
    input_grad = jnp.einsum(
        "ecr,ecf->rf", chosen_half, home[:, :capacity], preferred_element_type=f32
    ).astype(bf16)
    per_expert = jnp.einsum("ecr,ec->re", chosen, home[:, capacity, :capacity].astype(f32))
    route_grad = jnp.einsum("rke,re->rk", route_hits, per_expert).astype(bf16)
    return (input_grad, route_grad, grad_gate[None], grad_up[None], grad_down[None])


def solution(mesh):
    in_specs = (
        P(("dp", "expert"), "tensor"),
        P(("dp", "expert"), "tensor"),
        P(("dp", "expert"), None),
        P(("dp", "expert"), None),
        P(("dp", "expert")),
        P(),
        P(),
        P("expert", None, ("dp", "tensor")),
        P("expert", None, ("dp", "tensor")),
        P("expert", ("dp", "tensor"), None),
    )
    out_specs = (
        P(("dp", "expert"), "tensor"),
        P(("dp", "expert"), None),
        P("expert", None, ("dp", "tensor")),
        P("expert", None, ("dp", "tensor")),
        P("expert", ("dp", "tensor"), None),
    )
    return jax.shard_map(shards, mesh=mesh, in_specs=in_specs, out_specs=out_specs, check_vma=False)
```

```python
import jax
import jax.numpy as jnp
from jax import lax
from jax.sharding import PartitionSpec as P


def advantages(row_rollout, group_ids, rewards):
    same_group = (group_ids[:, None] == group_ids[None, :]).astype(jnp.float32)
    reward_values = rewards.astype(jnp.float32)
    group_total = jnp.dot(same_group, reward_values, precision=lax.Precision.HIGHEST)
    group_count = jnp.sum(same_group, axis=1)
    per_rollout = reward_values - group_total / group_count
    member = (
        row_rollout[:, None] == jnp.arange(per_rollout.shape[0], dtype=jnp.int32)[None, :]
    ).astype(jnp.float32)
    return jnp.dot(member, per_rollout, precision=lax.Precision.HIGHEST)


def selection(routing, probs, experts, capacity):
    route_hits = (
        routing[:, :, None] == jnp.arange(experts, dtype=jnp.int32)[None, None, :]
    ).astype(jnp.float32)
    occupied = jnp.sum(route_hits, axis=1)
    weight = jnp.einsum("rke,rk->re", route_hits, probs.astype(jnp.float32))
    before = jnp.cumsum(occupied, axis=0) - occupied
    slot_index = jnp.arange(capacity, dtype=jnp.float32)
    chosen = occupied.T[:, None, :] * (before.T[:, None, :] == slot_index[None, :, None]).astype(
        jnp.float32
    )
    return (route_hits, weight, chosen)


def shards(tokens, upstream, probs, routing, row_rollout, group_ids, rewards, w_gate, w_up, w_down):
    f32 = jnp.float32
    bf16 = jnp.bfloat16
    experts = lax.axis_size("expert")
    dp_size = lax.axis_size("dp")
    tensor_size = lax.axis_size("tensor")
    group_rows, features = tokens.shape
    routes_per_row = routing.shape[1]
    capacity = min(group_rows, 5 * group_rows * routes_per_row // (4 * experts))
    slots = experts * capacity

    advantage = advantages(row_rollout, group_ids, rewards)
    cotangent = (advantage[:, None] * upstream.astype(f32)).astype(bf16)
    route_hits, weight, chosen = selection(routing, probs, experts, capacity)
    chosen_half = chosen.astype(bf16)

    both = jnp.stack([tokens, cotangent])
    packed = jnp.einsum(
        "ecr,arf->aecf", chosen_half, both, preferred_element_type=f32
    ).astype(bf16)
    packed_prob = jnp.einsum("ecr,re->ec", chosen, weight).astype(bf16)
    prob_row = jnp.zeros((experts, 1, features), bf16).at[:, 0, :capacity].set(packed_prob)
    chunk = slots + 8
    all_rows = dp_size * chunk
    extra = jnp.zeros((chunk - slots, features), bf16)
    tok_pack = jnp.concatenate([packed[0], prob_row], axis=1)
    arrived_tok = lax.all_to_all(tok_pack, "expert", split_axis=0, concat_axis=0, tiled=True)
    extra_prob = extra.at[0, :slots].set(arrived_tok[:, capacity, :capacity].reshape(slots))
    tok_rows = jnp.concatenate([arrived_tok[:, :capacity].reshape(slots, features), extra_prob])
    tok_rows, cot_pack = lax.optimization_barrier((tok_rows, packed[1]))
    arrived_cot = lax.all_to_all(cot_pack, "expert", split_axis=0, concat_axis=0, tiled=True)
    cot_rows = jnp.concatenate([arrived_cot.reshape(slots, features), extra])

    g_tok = lax.all_gather(tok_rows, ("tensor", "dp"), axis=0, tiled=True)
    g_tok = g_tok.reshape(tensor_size, all_rows, features)
    g_cot = lax.all_gather(cot_rows, ("tensor", "dp"), axis=0, tiled=True)
    g_cot = g_cot.reshape(tensor_size, all_rows, features)
    slot_prob = g_tok[0].reshape(dp_size, chunk, features)[:, slots, :chunk].reshape(all_rows)

    wg = w_gate[0].reshape(tensor_size, features, -1)
    wu = w_up[0].reshape(tensor_size, features, -1)
    wd = w_down[0]
    hidden_width = wd.shape[0]
    wd = wd.reshape(hidden_width, tensor_size, features)

    w_in = jnp.concatenate([wg, wu], axis=2)
    gate_up = sum(
        jnp.dot(g_tok[t], w_in[t], preferred_element_type=f32) for t in range(tensor_size)
    )
    gate = gate_up[:, :hidden_width]
    up_part = gate_up[:, hidden_width:]
    back_hidden = sum(
        jnp.einsum("sf,hf->sh", g_cot[t], wd[:, t], preferred_element_type=f32)
        for t in range(tensor_size)
    )

    sigmoid_gate = jax.nn.sigmoid(gate)
    active = gate * sigmoid_gate
    hidden = (active * up_part).astype(bf16)
    hidden_wide = lax.optimization_barrier(hidden).astype(f32)
    route_part = jnp.sum(hidden_wide * back_hidden, axis=-1)
    scale = slot_prob.astype(f32)[:, None]
    scaled = scale * back_hidden
    grad_g = (scaled * up_part * sigmoid_gate * (1.0 + gate * (1.0 - sigmoid_gate))).astype(bf16)
    grad_u = (scaled * active).astype(bf16)
    weighted = (scale * hidden_wide).astype(bf16)

    grad_down = jnp.concatenate(
        [
            jnp.dot(weighted.T, g_cot[t], preferred_element_type=f32).astype(bf16)
            for t in range(tensor_size)
        ],
        axis=1,
    )
    grad_gate = jnp.concatenate(
        [
            jnp.dot(g_tok[t].T, grad_g, preferred_element_type=f32).astype(bf16)
            for t in range(tensor_size)
        ],
        axis=0,
    )
    grad_up = jnp.concatenate(
        [
            jnp.dot(g_tok[t].T, grad_u, preferred_element_type=f32).astype(bf16)
            for t in range(tensor_size)
        ],
        axis=0,
    )

    route_hi = route_part.astype(bf16).reshape(dp_size, chunk)
    route_lo = (route_part.reshape(dp_size, chunk) - route_hi.astype(f32)).astype(bf16)
    carry = jnp.zeros((dp_size, chunk, hidden_width), bf16)
    carry = carry.at[:, slots, :chunk].set(route_hi).at[:, slots + 1, :chunk].set(route_lo)
    lhs = jnp.concatenate([grad_g, grad_u, carry.reshape(all_rows, hidden_width)], axis=1)
    eye = (
        lax.broadcasted_iota(jnp.int32, (features, hidden_width), 0)
        == lax.broadcasted_iota(jnp.int32, (features, hidden_width), 1)
    ).astype(bf16)
    w_out = jnp.concatenate([wg, wu, jnp.broadcast_to(eye, wg.shape)], axis=2)
    product = jnp.einsum("sk,tfk->tsf", lhs, w_out, preferred_element_type=f32).astype(bf16)
    product = product.reshape(tensor_size * all_rows, features)
    own_rows = lax.psum_scatter(product, ("tensor", "dp"), scatter_dimension=0, tiled=True)
    own_rows, grad_gate, grad_up, grad_down = lax.optimization_barrier(
        (own_rows, grad_gate, grad_up, grad_down)
    )

    own_route = (
        own_rows[slots, :slots].astype(f32) + own_rows[slots + 1, :slots].astype(f32)
    ).astype(bf16)
    partner = lax.ppermute(own_route, "tensor", [(i, i ^ 1) for i in range(tensor_size)])
    own_route = jnp.where(lax.axis_index("tensor") == 0, own_route, partner)
    route_row = jnp.zeros((experts, 1, features), bf16).at[:, 0, :capacity].set(
        own_route.reshape(experts, capacity)
    )
    back_pack = jnp.concatenate(
        [own_rows[:slots].reshape(experts, capacity, features), route_row], axis=1
    )
    home = lax.all_to_all(back_pack, "expert", split_axis=0, concat_axis=0, tiled=True)
    input_grad = jnp.einsum(
        "ecr,ecf->rf", chosen_half, home[:, :capacity], preferred_element_type=f32
    ).astype(bf16)
    per_expert = jnp.einsum("ecr,ec->re", chosen, home[:, capacity, :capacity].astype(f32))
    route_grad = jnp.einsum("rke,re->rk", route_hits, per_expert).astype(bf16)
    return (input_grad, route_grad, grad_gate[None], grad_up[None], grad_down[None])


def solution(mesh):
    in_specs = (
        P(("dp", "expert"), "tensor"),
        P(("dp", "expert"), "tensor"),
        P(("dp", "expert"), None),
        P(("dp", "expert"), None),
        P(("dp", "expert")),
        P(),
        P(),
        P("expert", None, ("dp", "tensor")),
        P("expert", None, ("dp", "tensor")),
        P("expert", ("dp", "tensor"), None),
    )
    out_specs = (
        P(("dp", "expert"), "tensor"),
        P(("dp", "expert"), None),
        P("expert", None, ("dp", "tensor")),
        P("expert", None, ("dp", "tensor")),
        P("expert", ("dp", "tensor"), None),
    )
    return jax.shard_map(shards, mesh=mesh, in_specs=in_specs, out_specs=out_specs, check_vma=False)
```

```python
import jax
import jax.numpy as jnp
from jax import lax
from jax.sharding import PartitionSpec as P


def advantages(row_rollout, group_ids, rewards):
    same_group = (group_ids[:, None] == group_ids[None, :]).astype(jnp.float32)
    reward_values = rewards.astype(jnp.float32)
    group_total = jnp.dot(same_group, reward_values, precision=lax.Precision.HIGHEST)
    group_count = jnp.sum(same_group, axis=1)
    per_rollout = reward_values - group_total / group_count
    member = (
        row_rollout[:, None] == jnp.arange(per_rollout.shape[0], dtype=jnp.int32)[None, :]
    ).astype(jnp.float32)
    return jnp.dot(member, per_rollout, precision=lax.Precision.HIGHEST)


def selection(routing, probs, experts, capacity):
    route_hits = (
        routing[:, :, None] == jnp.arange(experts, dtype=jnp.int32)[None, None, :]
    ).astype(jnp.float32)
    occupied = jnp.sum(route_hits, axis=1)
    weight = jnp.einsum("rke,rk->re", route_hits, probs.astype(jnp.float32))
    before = jnp.cumsum(occupied, axis=0) - occupied
    slot_index = jnp.arange(capacity, dtype=jnp.float32)
    chosen = occupied.T[:, None, :] * (before.T[:, None, :] == slot_index[None, :, None]).astype(
        jnp.float32
    )
    return (route_hits, weight, chosen)


def shards(tokens, upstream, probs, routing, row_rollout, group_ids, rewards, w_gate, w_up, w_down):
    f32 = jnp.float32
    bf16 = jnp.bfloat16
    experts = lax.axis_size("expert")
    dp_size = lax.axis_size("dp")
    tensor_size = lax.axis_size("tensor")
    group_rows, features = tokens.shape
    routes_per_row = routing.shape[1]
    capacity = min(group_rows, 5 * group_rows * routes_per_row // (4 * experts))
    slots = experts * capacity

    advantage = advantages(row_rollout, group_ids, rewards)
    cotangent = (advantage[:, None] * upstream.astype(f32)).astype(bf16)
    route_hits, weight, chosen = selection(routing, probs, experts, capacity)
    chosen_half = chosen.astype(bf16)

    both = jnp.stack([tokens, cotangent])
    packed = jnp.einsum(
        "ecr,arf->aecf", chosen_half, both, preferred_element_type=f32
    ).astype(bf16)
    packed_prob = jnp.einsum("ecr,re->ec", chosen, weight).astype(bf16)
    prob_row = jnp.zeros((experts, 1, features), bf16).at[:, 0, :capacity].set(packed_prob)
    chunk = slots + 8
    all_rows = dp_size * chunk
    extra = jnp.zeros((chunk - slots, features), bf16)
    tok_pack = jnp.concatenate([packed[0], prob_row], axis=1)
    arrived_tok = lax.all_to_all(tok_pack, "expert", split_axis=0, concat_axis=0, tiled=True)
    extra_prob = extra.at[0, :slots].set(arrived_tok[:, capacity, :capacity].reshape(slots))
    tok_rows = jnp.concatenate([arrived_tok[:, :capacity].reshape(slots, features), extra_prob])
    tok_rows, cot_pack = lax.optimization_barrier((tok_rows, packed[1]))
    arrived_cot = lax.all_to_all(cot_pack, "expert", split_axis=0, concat_axis=0, tiled=True)
    cot_rows = jnp.concatenate([arrived_cot.reshape(slots, features), extra])

    g_tok = lax.all_gather(tok_rows, ("tensor", "dp"), axis=0, tiled=True)
    g_tok = g_tok.reshape(tensor_size, all_rows, features)
    g_cot = lax.all_gather(cot_rows, ("tensor", "dp"), axis=0, tiled=True)
    g_cot = g_cot.reshape(tensor_size, all_rows, features)
    slot_prob = g_tok[0].reshape(dp_size, chunk, features)[:, slots, :chunk].reshape(all_rows)

    wg = w_gate[0].reshape(tensor_size, features, -1)
    wu = w_up[0].reshape(tensor_size, features, -1)
    wd = w_down[0]
    hidden_width = wd.shape[0]
    wd = wd.reshape(hidden_width, tensor_size, features)

    w_in = jnp.concatenate([wg, wu], axis=2)
    gate_up = sum(
        jnp.dot(g_tok[t], w_in[t], preferred_element_type=f32) for t in range(tensor_size)
    )
    gate = gate_up[:, :hidden_width]
    up_part = gate_up[:, hidden_width:]
    back_hidden = sum(
        jnp.einsum("sf,hf->sh", g_cot[t], wd[:, t], preferred_element_type=f32)
        for t in range(tensor_size)
    )

    sigmoid_gate = jax.nn.sigmoid(gate)
    active = gate * sigmoid_gate
    hidden = (active * up_part).astype(bf16)
    hidden_wide = lax.optimization_barrier(hidden).astype(f32)
    route_part = jnp.sum(hidden_wide * back_hidden, axis=-1)
    scale = slot_prob.astype(f32)[:, None]
    scaled = scale * back_hidden
    grad_g = (scaled * up_part * sigmoid_gate * (1.0 + gate * (1.0 - sigmoid_gate))).astype(bf16)
    grad_u = (scaled * active).astype(bf16)
    weighted = (scale * hidden_wide).astype(bf16)

    grad_down = jnp.concatenate(
        [
            jnp.dot(weighted.T, g_cot[t], preferred_element_type=f32).astype(bf16)
            for t in range(tensor_size)
        ],
        axis=1,
    )
    grad_gate = jnp.concatenate(
        [
            jnp.dot(g_tok[t].T, grad_g, preferred_element_type=f32).astype(bf16)
            for t in range(tensor_size)
        ],
        axis=0,
    )
    grad_up = jnp.concatenate(
        [
            jnp.dot(g_tok[t].T, grad_u, preferred_element_type=f32).astype(bf16)
            for t in range(tensor_size)
        ],
        axis=0,
    )

    route_hi = route_part.astype(bf16).reshape(dp_size, chunk)
    route_lo = (route_part.reshape(dp_size, chunk) - route_hi.astype(f32)).astype(bf16)
    carry = jnp.zeros((dp_size, chunk, hidden_width), bf16)
    carry = carry.at[:, slots, :chunk].set(route_hi).at[:, slots + 1, :chunk].set(route_lo)
    lhs = jnp.concatenate([grad_g, grad_u, carry.reshape(all_rows, hidden_width)], axis=1)
    eye = (
        lax.broadcasted_iota(jnp.int32, (features, hidden_width), 0)
        == lax.broadcasted_iota(jnp.int32, (features, hidden_width), 1)
    ).astype(bf16)
    w_out = jnp.concatenate([wg, wu, jnp.broadcast_to(eye, wg.shape)], axis=2)
    product = jnp.einsum("sk,tfk->tsf", lhs, w_out, preferred_element_type=f32).astype(bf16)
    product = product.reshape(tensor_size * all_rows, features)
    own_rows = lax.psum_scatter(product, ("tensor", "dp"), scatter_dimension=0, tiled=True)
    own_rows, grad_gate, grad_up, grad_down = lax.optimization_barrier(
        (own_rows, grad_gate, grad_up, grad_down)
    )

    own_route = (
        own_rows[slots, :slots].astype(f32) + own_rows[slots + 1, :slots].astype(f32)
    ).astype(bf16)
    route_row = jnp.zeros((experts, 1, features), bf16).at[:, 0, :capacity].set(
        own_route.reshape(experts, capacity)
    )
    back_pack = jnp.concatenate(
        [own_rows[:slots].reshape(experts, capacity, features), route_row], axis=1
    )
    home = lax.all_to_all(back_pack, "expert", split_axis=0, concat_axis=0, tiled=True)
    input_grad = jnp.einsum(
        "ecr,ecf->rf", chosen_half, home[:, :capacity], preferred_element_type=f32
    ).astype(bf16)
    per_expert = jnp.einsum("ecr,ec->re", chosen, home[:, capacity, :capacity].astype(f32))
    route_grad = jnp.einsum("rke,re->rk", route_hits, per_expert).astype(bf16)
    partner = lax.ppermute(route_grad, "tensor", [(i, i ^ 1) for i in range(tensor_size)])
    route_grad = jnp.where(lax.axis_index("tensor") == 0, route_grad, partner)
    return (input_grad, route_grad, grad_gate[None], grad_up[None], grad_down[None])


def solution(mesh):
    in_specs = (
        P(("dp", "expert"), "tensor"),
        P(("dp", "expert"), "tensor"),
        P(("dp", "expert"), None),
        P(("dp", "expert"), None),
        P(("dp", "expert")),
        P(),
        P(),
        P("expert", None, ("dp", "tensor")),
        P("expert", None, ("dp", "tensor")),
        P("expert", ("dp", "tensor"), None),
    )
    out_specs = (
        P(("dp", "expert"), "tensor"),
        P(("dp", "expert"), None),
        P("expert", None, ("dp", "tensor")),
        P("expert", None, ("dp", "tensor")),
        P("expert", ("dp", "tensor"), None),
    )
    return jax.shard_map(shards, mesh=mesh, in_specs=in_specs, out_specs=out_specs, check_vma=False)
```

```python
import jax
import jax.numpy as jnp
from jax import lax
from jax.sharding import PartitionSpec as P


def advantages(row_rollout, group_ids, rewards):
    same_group = (group_ids[:, None] == group_ids[None, :]).astype(jnp.float32)
    reward_values = rewards.astype(jnp.float32)
    group_total = jnp.dot(same_group, reward_values, precision=lax.Precision.HIGHEST)
    group_count = jnp.sum(same_group, axis=1)
    per_rollout = reward_values - group_total / group_count
    member = (
        row_rollout[:, None] == jnp.arange(per_rollout.shape[0], dtype=jnp.int32)[None, :]
    ).astype(jnp.float32)
    return jnp.dot(member, per_rollout, precision=lax.Precision.HIGHEST)


def selection(routing, probs, experts, capacity):
    route_hits = (
        routing[:, :, None] == jnp.arange(experts, dtype=jnp.int32)[None, None, :]
    ).astype(jnp.float32)
    occupied = jnp.sum(route_hits, axis=1)
    weight = jnp.einsum("rke,rk->re", route_hits, probs.astype(jnp.float32))
    before = jnp.cumsum(occupied, axis=0) - occupied
    slot_index = jnp.arange(capacity, dtype=jnp.float32)
    chosen = occupied.T[:, None, :] * (before.T[:, None, :] == slot_index[None, :, None]).astype(
        jnp.float32
    )
    return (route_hits, weight, chosen)


def shards(tokens, upstream, probs, routing, row_rollout, group_ids, rewards, w_gate, w_up, w_down):
    f32 = jnp.float32
    bf16 = jnp.bfloat16
    experts = lax.axis_size("expert")
    dp_size = lax.axis_size("dp")
    tensor_size = lax.axis_size("tensor")
    group_rows, features = tokens.shape
    routes_per_row = routing.shape[1]
    capacity = min(group_rows, 5 * group_rows * routes_per_row // (4 * experts))
    slots = experts * capacity

    advantage = advantages(row_rollout, group_ids, rewards)
    cotangent = (advantage[:, None] * upstream.astype(f32)).astype(bf16)
    route_hits, weight, chosen = selection(routing, probs, experts, capacity)
    chosen_half = chosen.astype(bf16)

    both = jnp.stack([tokens, cotangent])
    packed = jnp.einsum(
        "ecr,arf->aecf", chosen_half, both, preferred_element_type=f32
    ).astype(bf16)
    packed_prob = jnp.einsum("ecr,re->ec", chosen, weight).astype(bf16)
    prob_row = jnp.zeros((experts, 1, features), bf16).at[:, 0, :capacity].set(packed_prob)
    chunk = slots + 8
    all_rows = dp_size * chunk
    extra = jnp.zeros((chunk - slots, features), bf16)
    tok_pack = jnp.concatenate([packed[0], prob_row], axis=1)
    arrived_tok = lax.all_to_all(tok_pack, "expert", split_axis=0, concat_axis=0, tiled=True)
    extra_prob = extra.at[0, :slots].set(arrived_tok[:, capacity, :capacity].reshape(slots))
    tok_rows = jnp.concatenate([arrived_tok[:, :capacity].reshape(slots, features), extra_prob])
    tok_rows, cot_pack = lax.optimization_barrier((tok_rows, packed[1]))
    arrived_cot = lax.all_to_all(cot_pack, "expert", split_axis=0, concat_axis=0, tiled=True)
    cot_rows = jnp.concatenate([arrived_cot.reshape(slots, features), extra])

    g_tok = lax.all_gather(tok_rows, ("tensor", "dp"), axis=0, tiled=True)
    g_tok = g_tok.reshape(tensor_size, all_rows, features)
    g_cot = lax.all_gather(cot_rows, ("tensor", "dp"), axis=0, tiled=True)
    g_cot = g_cot.reshape(tensor_size, all_rows, features)
    slot_prob = g_tok[0].reshape(dp_size, chunk, features)[:, slots, :chunk].reshape(all_rows)

    wg = w_gate[0].reshape(tensor_size, features, -1)
    wu = w_up[0].reshape(tensor_size, features, -1)
    wd = w_down[0]
    hidden_width = wd.shape[0]
    wd = wd.reshape(hidden_width, tensor_size, features)

    w_in = jnp.concatenate([wg, wu], axis=2)
    gate_up = sum(
        jnp.dot(g_tok[t], w_in[t], preferred_element_type=f32) for t in range(tensor_size)
    )
    gate = gate_up[:, :hidden_width]
    up_part = gate_up[:, hidden_width:]
    back_hidden = jnp.einsum("tsf,htf->sh", g_cot, wd, preferred_element_type=f32)

    sigmoid_gate = jax.nn.sigmoid(gate)
    active = gate * sigmoid_gate
    hidden = (active * up_part).astype(bf16)
    hidden_wide = lax.optimization_barrier(hidden).astype(f32)
    route_part = jnp.sum(hidden_wide * back_hidden, axis=-1)
    scale = slot_prob.astype(f32)[:, None]
    scaled = scale * back_hidden
    grad_g = (scaled * up_part * sigmoid_gate * (1.0 + gate * (1.0 - sigmoid_gate))).astype(bf16)
    grad_u = (scaled * active).astype(bf16)
    weighted = (scale * hidden_wide).astype(bf16)

    grad_down = jnp.concatenate(
        [
            jnp.dot(weighted.T, g_cot[t], preferred_element_type=f32).astype(bf16)
            for t in range(tensor_size)
        ],
        axis=1,
    )
    grad_gate = jnp.concatenate(
        [
            jnp.dot(g_tok[t].T, grad_g, preferred_element_type=f32).astype(bf16)
            for t in range(tensor_size)
        ],
        axis=0,
    )
    grad_up = jnp.concatenate(
        [
            jnp.dot(g_tok[t].T, grad_u, preferred_element_type=f32).astype(bf16)
            for t in range(tensor_size)
        ],
        axis=0,
    )

    route_hi = route_part.astype(bf16).reshape(dp_size, chunk)
    route_lo = (route_part.reshape(dp_size, chunk) - route_hi.astype(f32)).astype(bf16)
    carry = jnp.zeros((dp_size, chunk, hidden_width), bf16)
    carry = carry.at[:, slots, :chunk].set(route_hi).at[:, slots + 1, :chunk].set(route_lo)
    lhs = jnp.concatenate([grad_g, grad_u, carry.reshape(all_rows, hidden_width)], axis=1)
    eye = (
        lax.broadcasted_iota(jnp.int32, (features, hidden_width), 0)
        == lax.broadcasted_iota(jnp.int32, (features, hidden_width), 1)
    ).astype(bf16)
    w_out = jnp.concatenate([wg, wu, jnp.broadcast_to(eye, wg.shape)], axis=2)
    product = jnp.einsum("sk,tfk->tsf", lhs, w_out, preferred_element_type=f32).astype(bf16)
    product = product.reshape(tensor_size * all_rows, features)
    own_rows = lax.psum_scatter(product, ("tensor", "dp"), scatter_dimension=0, tiled=True)
    own_rows, grad_gate, grad_up, grad_down = lax.optimization_barrier(
        (own_rows, grad_gate, grad_up, grad_down)
    )

    own_route = (
        own_rows[slots, :slots].astype(f32) + own_rows[slots + 1, :slots].astype(f32)
    ).astype(bf16)
    partner = lax.ppermute(own_route, "tensor", [(i, i ^ 1) for i in range(tensor_size)])
    own_route = jnp.where(lax.axis_index("tensor") == 0, own_route, partner)
    route_row = jnp.zeros((experts, 1, features), bf16).at[:, 0, :capacity].set(
        own_route.reshape(experts, capacity)
    )
    back_pack = jnp.concatenate(
        [own_rows[:slots].reshape(experts, capacity, features), route_row], axis=1
    )
    home = lax.all_to_all(back_pack, "expert", split_axis=0, concat_axis=0, tiled=True)
    input_grad = jnp.einsum(
        "ecr,ecf->rf", chosen_half, home[:, :capacity], preferred_element_type=f32
    ).astype(bf16)
    per_expert = jnp.einsum("ecr,ec->re", chosen, home[:, capacity, :capacity].astype(f32))
    route_grad = jnp.einsum("rke,re->rk", route_hits, per_expert).astype(bf16)
    return (input_grad, route_grad, grad_gate[None], grad_up[None], grad_down[None])


def solution(mesh):
    in_specs = (
        P(("dp", "expert"), "tensor"),
        P(("dp", "expert"), "tensor"),
        P(("dp", "expert"), None),
        P(("dp", "expert"), None),
        P(("dp", "expert")),
        P(),
        P(),
        P("expert", None, ("dp", "tensor")),
        P("expert", None, ("dp", "tensor")),
        P("expert", ("dp", "tensor"), None),
    )
    out_specs = (
        P(("dp", "expert"), "tensor"),
        P(("dp", "expert"), None),
        P("expert", None, ("dp", "tensor")),
        P("expert", None, ("dp", "tensor")),
        P("expert", ("dp", "tensor"), None),
    )
    return jax.shard_map(shards, mesh=mesh, in_specs=in_specs, out_specs=out_specs, check_vma=False)
```
